32 devices in a mesh: groups: 2 (over y), lat: 16 (over z, x, core).
Axes of the slice: x: 2, y: 2, z: 4, core: 2. Of those that a mesh axis runs over, the one named last changes fastest.
Arguments:
- latent: bfloat16 [16384, 1536], P(('groups', 'lat')), parts along dimension 0, may hold values from -400 to 400
- query_gain: float32 [1536], replicated, may hold values from 0.1 to 1.9
- key_gain: float32 [1536], replicated, may hold values from 0.1 to 1.9
- output_gain: float32 [1536], replicated, may hold values from 0.1 to 1.9
- output_weight: bfloat16 [1536, 1536], replicated, may hold values from -0.15625 to 0.15625
- observations: bfloat16 [128, 128, 128], P(('groups', 'lat')), parts along dimension 0, may hold values from -6 to 6
- panels: bfloat16 [1024, 1536], P('lat'), may hold values from -0.5 to 0.5
- instrument: int32 [128], P('groups'), parts along dimension 0, may hold values from 0 to 7
- observed_count: int32 [128], P('groups'), parts along dimension 0, may hold values from 1 to 128
- footprint: int32 [128, 6], P(('groups', 'lat')), parts along dimension 0, may hold values from 0 to 63, as said below
- tile_blocks: int32 [128], P(('groups', 'lat')), parts along dimension 0, may hold values from 1 to 6
Outputs:
- encoded: bfloat16 [16384, 1536], P(('groups', 'lat')), parts along dimension 0
The draws below stay inside these ranges and needn't reach their ends.
There are 2 independent parts, one for each index of `groups`. The reference program is written for one: setup_inputs(seed, part) draws one part's arguments, and reference() takes and returns one part's arrays. A program takes and returns all parts, laid end to end along the dimension named above; an argument that names none is the same for every part. Nothing has to cross between parts.
Inputs may be any that keep to these rules, and one draw needn't show every extreme that they name: `footprint`: tile t lies on latitude device t // 4 and block b on b // 4; every entry of tile t's list names a block on that device or on one of the two beside it.
All inputs are finite; a program needn't handle non-finite values.
Results may differ from the reference program's by a relative error of at most 0.0039.
Values may be sent and summed in bfloat16 or wider, within the bound.
No kernel may reach another device: no remote copies, remote signals or barrier semaphores. Data moves between devices by JAX's collectives and lax.ppermute only.
A program may use at most 128 MiB of HBM per device.

```python
import math
import jax
import jax.numpy as jnp
from jax import lax

D = 1536
HD = 64
NINST = 8
CH = 128
CELLS = 128
OBS = 128
MAXB = 6
TILE_DEV = 4
BLK_DEV = 4
NTILE = 64
ROWS = 8192
NBLK = 64
PROWS = 1024


def draw_latent(key, part):
    first = jax.random.fold_in(key, 0)
    values = jax.random.normal(first, (ROWS, D), jnp.float32)
    values = jnp.clip(values, -6.0, 6.0)
    return values.astype(jnp.bfloat16)


def draw_observed_count(key, part):
    first, second = jax.random.split(key, 2)
    counts = jax.random.randint(first, (NBLK,), 1, OBS + 1, jnp.int32)
    where_full = jax.random.randint(second, (), 0, NBLK, jnp.int32)
    counts = counts.at[where_full].set(OBS)
    counts = counts.at[(where_full + 1) % NBLK].set(1)
    return counts


def draw_tile_blocks(key, part):
    first, second, third, fourth = jax.random.split(key, 4)
    devices = NTILE // TILE_DEV
    heavy = jax.random.randint(first, (devices,), 0, 4, jnp.int32) == 0
    chosen = jax.random.randint(second, (), 0, devices, jnp.int32)
    heavy = heavy.at[chosen].set(True)
    heavy = heavy.at[(chosen + 1) % devices].set(False)
    owner = jnp.arange(NTILE, dtype=jnp.int32) // TILE_DEV
    light_counts = jax.random.randint(third, (NTILE,), 1, 3, jnp.int32)
    heavy_counts = jax.random.randint(fourth, (NTILE,), MAXB - 1, MAXB + 1, jnp.int32)
    counts = jnp.minimum(jnp.where(heavy[owner], heavy_counts, light_counts), MAXB)
    counts = counts.at[chosen * TILE_DEV].set(MAXB)
    counts = counts.at[(chosen + 1) % devices * TILE_DEV].set(1)
    return counts


def draw_footprint(key, part):
    first, second = jax.random.split(jax.random.fold_in(key, 7), 2)
    devices = NTILE // TILE_DEV
    owner = jnp.arange(NTILE, dtype=jnp.int32) // TILE_DEV
    offsets = jax.random.randint(first, (NTILE, MAXB), -1, 2, jnp.int32)
    source = jnp.clip(owner[:, None] + offsets, 0, devices - 1)
    within = jax.random.randint(second, (NTILE, MAXB), 0, BLK_DEV, jnp.int32)
    return source * BLK_DEV + within


def place_ends(drawn, stream_key, smallest, high):
    spot = [jax.random.randint(jax.random.fold_in(stream_key, axis), (), 0, length) for axis, length in enumerate(drawn.shape)]
    longest = drawn.shape.index(max(drawn.shape))
    neighbour = spot[:longest] + [(spot[longest] + 1) % drawn.shape[longest]] + spot[longest + 1:]
    return drawn.at[tuple(spot)].set(smallest).at[tuple(neighbour)].set(high)


def levels(key, extent, cuts, smallest, high):
    def one(position, parts):
        heights = jax.random.uniform(jax.random.fold_in(jax.random.fold_in(key, 6), position), (parts,), jnp.float32, smallest / len(cuts), high / len(cuts))
        return jnp.repeat(jnp.exp(heights), extent[position] // parts).reshape((-1,) + (1,) * (len(extent) - position - 1))

    factor_of = one(*cuts[0])
    for cut in cuts[1:]:
        factor_of = factor_of * one(*cut)
    return factor_of


def bell_draw(own_key, shape, scale, most, shards=(), kind=jnp.bfloat16):
    factor_of = levels(own_key, shape, shards, -0.22, 0.18) if shards else 1.0
    array = jax.random.normal(own_key, shape, jnp.float32) * scale * factor_of
    return jnp.minimum(jnp.maximum(array, -most), most).astype(kind)


def setup_inputs(seed: int = 0, part: int = 0) -> dict:
    key_list = jax.random.split(jax.random.key(seed), 12)
    part_splits = jax.random.split(jax.random.fold_in(key_list[11], part), 12)
    return {
        "latent": draw_latent(jax.random.fold_in(jax.random.fold_in(key_list[11], part), 71), part),
        "query_gain": jnp.clip(1.0 + 0.18 * jax.random.normal(key_list[1], (D,), jnp.float32), 0.1, 1.9),
        "key_gain": jnp.clip(1.0 + 0.18 * jax.random.normal(key_list[2], (D,), jnp.float32), 0.1, 1.9),
        "output_gain": jnp.clip(1.0 + 0.18 * jax.random.normal(key_list[3], (D,), jnp.float32), 0.1, 1.9),
        "output_weight": bell_draw(key_list[4], (D, D), D ** -0.5, 0.15625),
        "observations": bell_draw(part_splits[5], (NBLK, OBS, CH), 1.0, 6.0, ((0, 16),)),
        "panels": bell_draw(key_list[6], (PROWS, D), CH ** -0.5, 0.5, ((0, 16),)),
        "instrument": place_ends(jax.random.randint(part_splits[7], (NBLK,), 0, NINST), jax.random.fold_in(part_splits[7], 1), 0, NINST - 1).astype(jnp.int32),
        "observed_count": draw_observed_count(jax.random.fold_in(jax.random.fold_in(key_list[11], part), 71), part),
        "footprint": draw_footprint(jax.random.fold_in(jax.random.fold_in(key_list[11], part), 71), part),
        "tile_blocks": draw_tile_blocks(jax.random.fold_in(jax.random.fold_in(key_list[11], part), 71), part),
    }


def normalize(values, gain):
    values = values.astype(jnp.float32)
    return values * lax.rsqrt(lax.optimization_barrier(jnp.mean(values * values, axis=-1, keepdims=True)) + 1e-06) * gain

def reference(latent, query_gain, key_gain, output_gain, output_weight, observations, panels, instrument, observed_count, footprint, tile_blocks):
    table = panels.reshape(NINST, CH, D)

    def embed_one(pair):
        block, kind = pair
        return jnp.dot(block, table[kind], preferred_element_type=jnp.float32).astype(jnp.bfloat16)
    embedded = lax.map(embed_one, (observations, instrument))
    keys = normalize(embedded, key_gain).astype(jnp.bfloat16)
    heads = D // HD
    queries = (latent.astype(jnp.float32) * query_gain).astype(jnp.bfloat16).reshape(NTILE, CELLS, heads, HD)
    scale = 1.0 / math.sqrt(HD)

    def tile_attend(item):
        tile_queries, chosen, used = item
        tile_keys = keys[chosen].reshape(MAXB * OBS, heads, HD).astype(jnp.float32)
        tile_values = embedded[chosen].reshape(MAXB * OBS, heads, HD).astype(jnp.float32)
        slot_ok = jnp.arange(MAXB, dtype=jnp.int32)[:, None] < used
        row_ok = jnp.arange(OBS, dtype=jnp.int32)[None, :] < observed_count[chosen][:, None]
        usable = (slot_ok & row_ok).reshape(MAXB * OBS)
        scores = jnp.einsum('qhd,khd->hqk', tile_queries.astype(jnp.float32), tile_keys) * scale
        highest = lax.optimization_barrier(jnp.max(jnp.where(usable, scores, -jnp.inf), axis=-1))
        weights = jnp.where(usable, jnp.exp(scores - highest[..., None]), 0.0)
        total = lax.optimization_barrier(jnp.sum(weights, axis=-1))
        rounded = lax.optimization_barrier(weights.astype(jnp.bfloat16)).astype(jnp.float32)
        summed = jnp.einsum('hqk,khd->qhd', rounded, tile_values)
        attended = summed / jnp.transpose(total)[..., None]
        return attended.reshape(CELLS, D).astype(jnp.bfloat16)
    attended = lax.map(tile_attend, (queries, footprint, tile_blocks)).reshape(ROWS, D)
    mixed = latent.astype(jnp.float32) + jnp.dot(attended, output_weight, preferred_element_type=jnp.float32)
    return normalize(mixed, output_gain).astype(jnp.bfloat16)
```

```python
import functools
import math

import jax
import jax.numpy as jnp
from jax import lax
from jax.experimental import pallas as pl
from jax.experimental.pallas import tpu as pltpu
from jax.sharding import PartitionSpec as P

D = 1536
HD = 64
CH = 128
CELLS = 128
OBS = 128
MAXB = 6
LANES = 128


def padded(value, axis, width):
    peers, length = lax.axis_size(axis), value.shape[0]
    up = [(i, i + 1) for i in range(peers - 1)]
    down = [(j, i) for i, j in up]
    before = lax.ppermute(value[length - width:], axis, up)
    after = lax.ppermute(value[:width], axis, down)
    return jnp.concatenate([before, value, after], axis=0)


def normalize(values, gain):
    values = values.astype(jnp.float32)
    return values * lax.rsqrt(jnp.mean(values * values, axis=-1, keepdims=True) + 1e-06) * gain


def attend_kernel(ids_ref, nb_ref, cnt_ref, q_ref, k_ref, v_ref, o_ref, s_ref, m_ref, t_ref, a_ref):
    tile = pl.program_id(0)
    used = nb_ref[tile]
    scale = 1.0 / math.sqrt(HD)
    lane = lax.broadcasted_iota(jnp.int32, (1, LANES), 1)
    low = lane < HD
    for pair in range(D // LANES):
        cols = pl.ds(pair * LANES, LANES)
        qp = q_ref[:, cols].astype(jnp.float32)
        qa = jnp.where(low, qp, 0.0).astype(jnp.bfloat16)
        qb = jnp.where(low, 0.0, qp).astype(jnp.bfloat16)
        m_ref[...] = jnp.full(m_ref.shape, -jnp.inf, jnp.float32)
        t_ref[...] = jnp.zeros(t_ref.shape, jnp.float32)
        a_ref[...] = jnp.zeros(a_ref.shape, jnp.float32)

        def score_step(j, carry):
            block = ids_ref[tile * MAXB + j]
            keys = k_ref[block, :, cols]
            valid = lane < cnt_ref[block]
            for h, qh in enumerate((qa, qb)):
                s = lax.dot_general(
                    qh, keys, (((1,), (1,)), ((), ())), preferred_element_type=jnp.float32
                ) * scale
                s = jnp.where(valid, s, -jnp.inf)
                s_ref[h, j] = s
                m_ref[h] = jnp.maximum(m_ref[h], s)
            return carry

        lax.fori_loop(0, used, score_step, 0)
        ma = jnp.max(m_ref[0], axis=1, keepdims=True)
        mb = jnp.max(m_ref[1], axis=1, keepdims=True)

        def value_step(j, carry):
            block = ids_ref[tile * MAXB + j]
            values = v_ref[block, :, cols]
            for h, mh in enumerate((ma, mb)):
                w = jnp.exp(s_ref[h, j] - mh)
                t_ref[h] = t_ref[h] + w
                a_ref[h] = a_ref[h] + jnp.dot(
                    w.astype(jnp.bfloat16), values, preferred_element_type=jnp.float32
                )
            return carry

        lax.fori_loop(0, used, value_step, 0)
        ta = jnp.sum(t_ref[0], axis=1, keepdims=True)
        tb = jnp.sum(t_ref[1], axis=1, keepdims=True)
        out = jnp.where(low, a_ref[0] / ta, a_ref[1] / tb)
        o_ref[:, cols] = out.astype(jnp.bfloat16)


def attend(local_ids, tile_blocks, counts, queries, keys, values):
    tiles = queries.shape[0] // CELLS
    near = keys.shape[0]
    grid_spec = pltpu.PrefetchScalarGridSpec(
        num_scalar_prefetch=3,
        grid=(tiles,),
        in_specs=[
            pl.BlockSpec((CELLS, D), lambda t, *_: (t, 0)),
            pl.BlockSpec((near, OBS, D), lambda t, *_: (0, 0, 0)),
            pl.BlockSpec((near, OBS, D), lambda t, *_: (0, 0, 0)),
        ],
        out_specs=pl.BlockSpec((CELLS, D), lambda t, *_: (t, 0)),
        scratch_shapes=[
            pltpu.VMEM((2, MAXB, CELLS, OBS), jnp.float32),
            pltpu.VMEM((2, CELLS, LANES), jnp.float32),
            pltpu.VMEM((2, CELLS, LANES), jnp.float32),
            pltpu.VMEM((2, CELLS, LANES), jnp.float32),
        ],
    )
    return pl.pallas_call(
        attend_kernel,
        grid_spec=grid_spec,
        out_shape=jax.ShapeDtypeStruct(queries.shape, jnp.bfloat16),
        compiler_params=pltpu.CompilerParams(vmem_limit_bytes=48 * 1024 * 1024),
    )(local_ids.reshape(-1), tile_blocks, counts, queries, keys, values)


def body(
    latent,
    query_gain,
    key_gain,
    output_gain,
    output_weight,
    observations,
    panels,
    instrument,
    observed_count,
    footprint,
    tile_blocks,
):
    block_count = observations.shape[0]
    position = lax.axis_index("lat")
    first_block = (position - 1) * block_count
    all_blocks = instrument.shape[0]
    table = lax.all_gather(panels, "lat", axis=0, tiled=True)
    kinds = table.shape[0] // CH
    near_obs = padded(observations, "lat", block_count)
    near_count = near_obs.shape[0]
    near_ids = jnp.clip(first_block + jnp.arange(near_count, dtype=jnp.int32), 0, all_blocks - 1)
    near_kinds = instrument[near_ids]
    counts = observed_count[near_ids]
    near_panels = table.reshape(kinds, CH, D)[near_kinds]
    embedded = jnp.einsum(
        "boc,bcd->bod", near_obs, near_panels, preferred_element_type=jnp.float32
    ).astype(jnp.bfloat16)
    keys = normalize(embedded, key_gain).astype(jnp.bfloat16)
    queries = (latent.astype(jnp.float32) * query_gain).astype(jnp.bfloat16)
    local_ids = (footprint - first_block).astype(jnp.int32)
    attended = attend(local_ids, tile_blocks.astype(jnp.int32), counts, queries, keys, embedded)
    mixed = latent.astype(jnp.float32) + jnp.dot(
        attended, output_weight, preferred_element_type=jnp.float32
    )
    return normalize(mixed, output_gain).astype(jnp.bfloat16)


def solution(mesh):
    return jax.shard_map(
        body,
        mesh=mesh,
        in_specs=(
            P(("groups", "lat"), None),
            P(),
            P(),
            P(),
            P(),
            P(("groups", "lat"), None, None),
            P("lat", None),
            P("groups"),
            P("groups"),
            P(("groups", "lat"), None),
            P(("groups", "lat")),
        ),
        out_specs=P(("groups", "lat"), None),
        check_vma=False,
    )
```

```python
import functools
import math

import jax
import jax.numpy as jnp
from jax import lax
from jax.experimental import pallas as pl
from jax.experimental.pallas import tpu as pltpu
from jax.sharding import PartitionSpec as P

D = 1536
HD = 64
CH = 128
CELLS = 128
OBS = 128
MAXB = 6
LANES = 128
LAT = ("chips", "core")


def padded(value, axis, width):
    peers, length = lax.axis_size(axis), value.shape[0]
    up = [(i, i + 1) for i in range(peers - 1)]
    down = [(j, i) for i, j in up]
    before = lax.ppermute(value[length - width:], axis, up)
    after = lax.ppermute(value[:width], axis, down)
    return jnp.concatenate([before, value, after], axis=0)


def normalize(values, gain):
    values = values.astype(jnp.float32)
    return values * lax.rsqrt(jnp.mean(values * values, axis=-1, keepdims=True) + 1e-06) * gain


def attend_kernel(ids_ref, nb_ref, cnt_ref, q_ref, k_ref, v_ref, o_ref, s_ref, m_ref, t_ref, a_ref):
    tile = pl.program_id(0)
    used = nb_ref[tile]
    scale = 1.0 / math.sqrt(HD)
    lane = lax.broadcasted_iota(jnp.int32, (1, LANES), 1)
    low = lane < HD
    for pair in range(D // LANES):
        cols = pl.ds(pair * LANES, LANES)
        qp = q_ref[:, cols].astype(jnp.float32)
        qa = jnp.where(low, qp, 0.0).astype(jnp.bfloat16)
        qb = jnp.where(low, 0.0, qp).astype(jnp.bfloat16)
        m_ref[...] = jnp.full(m_ref.shape, -jnp.inf, jnp.float32)
        t_ref[...] = jnp.zeros(t_ref.shape, jnp.float32)
        a_ref[...] = jnp.zeros(a_ref.shape, jnp.float32)

        def score_step(j, carry):
            block = ids_ref[tile * MAXB + j]
            keys = k_ref[block, :, cols]
            valid = lane < cnt_ref[block]
            for h, qh in enumerate((qa, qb)):
                s = lax.dot_general(
                    qh, keys, (((1,), (1,)), ((), ())), preferred_element_type=jnp.float32
                ) * scale
                s = jnp.where(valid, s, -jnp.inf)
                s_ref[h, j] = s
                m_ref[h] = jnp.maximum(m_ref[h], s)
            return carry

        lax.fori_loop(0, used, score_step, 0)
        ma = jnp.max(m_ref[0], axis=1, keepdims=True)
        mb = jnp.max(m_ref[1], axis=1, keepdims=True)

        def value_step(j, carry):
            block = ids_ref[tile * MAXB + j]
            values = v_ref[block, :, cols]
            for h, mh in enumerate((ma, mb)):
                w = jnp.exp(s_ref[h, j] - mh)
                t_ref[h] = t_ref[h] + w
                a_ref[h] = a_ref[h] + jnp.dot(
                    w.astype(jnp.bfloat16), values, preferred_element_type=jnp.float32
                )
            return carry

        lax.fori_loop(0, used, value_step, 0)
        ta = jnp.sum(t_ref[0], axis=1, keepdims=True)
        tb = jnp.sum(t_ref[1], axis=1, keepdims=True)
        out = jnp.where(low, a_ref[0] / ta, a_ref[1] / tb)
        o_ref[:, cols] = out.astype(jnp.bfloat16)


def attend(local_ids, tile_blocks, counts, queries, keys, values):
    tiles = queries.shape[0] // CELLS
    near = keys.shape[0]
    grid_spec = pltpu.PrefetchScalarGridSpec(
        num_scalar_prefetch=3,
        grid=(tiles,),
        in_specs=[
            pl.BlockSpec((CELLS, D), lambda t, *_: (t, 0)),
            pl.BlockSpec((near, OBS, D), lambda t, *_: (0, 0, 0)),
            pl.BlockSpec((near, OBS, D), lambda t, *_: (0, 0, 0)),
        ],
        out_specs=pl.BlockSpec((CELLS, D), lambda t, *_: (t, 0)),
        scratch_shapes=[
            pltpu.VMEM((2, MAXB, CELLS, OBS), jnp.float32),
            pltpu.VMEM((2, CELLS, LANES), jnp.float32),
            pltpu.VMEM((2, CELLS, LANES), jnp.float32),
            pltpu.VMEM((2, CELLS, LANES), jnp.float32),
        ],
    )
    return pl.pallas_call(
        attend_kernel,
        grid_spec=grid_spec,
        out_shape=jax.ShapeDtypeStruct(queries.shape, jnp.bfloat16),
        compiler_params=pltpu.CompilerParams(vmem_limit_bytes=48 * 1024 * 1024),
    )(local_ids.reshape(-1), tile_blocks, counts, queries, keys, values)


def body(
    latent,
    query_gain,
    key_gain,
    output_gain,
    output_weight,
    observations,
    panels,
    instrument,
    observed_count,
    footprint,
    tile_blocks,
):
    block_count = observations.shape[0]
    position = lax.axis_index(LAT)
    first_block = (position - 1) * block_count
    all_blocks = instrument.shape[0]
    part_rows = panels.shape[0]
    chips = lax.axis_size("chips")
    cores = lax.axis_size("core")
    per_core = lax.all_gather(panels, "chips", axis=0, tiled=True)
    table = lax.all_gather(per_core, "core", axis=0, tiled=True)
    near_obs = padded(observations, LAT, block_count)
    near_count = near_obs.shape[0]
    near_ids = jnp.clip(first_block + jnp.arange(near_count, dtype=jnp.int32), 0, all_blocks - 1)
    near_kinds = instrument[near_ids]
    counts = observed_count[near_ids]
    rows = near_kinds[:, None] * CH + jnp.arange(CH, dtype=jnp.int32)[None, :]
    piece, within = rows // part_rows, rows % part_rows
    rows = (piece % cores) * (chips * part_rows) + (piece // cores) * part_rows + within
    near_panels = table[rows]
    embedded = jnp.einsum(
        "boc,bcd->bod", near_obs, near_panels, preferred_element_type=jnp.float32
    ).astype(jnp.bfloat16)
    keys = normalize(embedded, key_gain).astype(jnp.bfloat16)
    queries = (latent.astype(jnp.float32) * query_gain).astype(jnp.bfloat16)
    local_ids = (footprint - first_block).astype(jnp.int32)
    attended = attend(local_ids, tile_blocks.astype(jnp.int32), counts, queries, keys, embedded)
    mixed = latent.astype(jnp.float32) + jnp.dot(
        attended, output_weight, preferred_element_type=jnp.float32
    )
    return normalize(mixed, output_gain).astype(jnp.bfloat16)


def solution(mesh):
    groups, lat = mesh.devices.shape
    cores = 2 if lat % 2 == 0 else 1
    split = jax.sharding.Mesh(mesh.devices.reshape(groups, lat // cores, cores), ("groups",) + LAT)
    return jax.shard_map(
        body,
        mesh=split,
        in_specs=(
            P(("groups",) + LAT, None),
            P(),
            P(),
            P(),
            P(),
            P(("groups",) + LAT, None, None),
            P(LAT, None),
            P("groups"),
            P("groups"),
            P(("groups",) + LAT, None),
            P(("groups",) + LAT),
        ),
        out_specs=P(("groups",) + LAT, None),
        check_vma=False,
    )
```

```python
import functools
import math

import jax
import jax.numpy as jnp
from jax import lax
from jax.experimental import pallas as pl
from jax.experimental.pallas import tpu as pltpu
from jax.sharding import PartitionSpec as P

D = 1536
HD = 64
CH = 128
CELLS = 128
OBS = 128
MAXB = 6
LANES = 128


def padded(value, axis, width):
    peers, length = lax.axis_size(axis), value.shape[0]
    up = [(i, i + 1) for i in range(peers - 1)]
    down = [(j, i) for i, j in up]
    before = lax.ppermute(value[length - width:], axis, up)
    after = lax.ppermute(value[:width], axis, down)
    return jnp.concatenate([before, value, after], axis=0)


def normalize(values, gain):
    values = values.astype(jnp.float32)
    return values * lax.rsqrt(jnp.mean(values * values, axis=-1, keepdims=True) + 1e-06) * gain


def attend_kernel(ids_ref, nb_ref, cnt_ref, qt_ref, k_ref, vt_ref, o_ref, s_ref):
    tile = pl.program_id(0)
    used = nb_ref[tile]
    scale = 1.0 / math.sqrt(HD)
    row = lax.broadcasted_iota(jnp.int32, (LANES, 1), 0)
    low = row < HD
    wide = 2 * LANES
    for pair in range(D // LANES):
        rows = pl.ds(pair * LANES, LANES)
        qt = qt_ref[0, rows, :].astype(jnp.float32)
        q2 = jnp.concatenate(
            [jnp.where(low, qt, 0.0), jnp.where(low, 0.0, qt)], axis=1
        ).astype(jnp.bfloat16)

        def score_step(j, high):
            block = ids_ref[tile * MAXB + j]
            keys = k_ref[block, :, rows]
            s = jnp.dot(keys, q2, preferred_element_type=jnp.float32) * scale
            s = jnp.where(row < cnt_ref[block], s, -jnp.inf)
            s_ref[j] = s
            return jnp.maximum(high, jnp.max(s, axis=0, keepdims=True))

        high = lax.fori_loop(
            0, used, score_step, jnp.full((1, wide), -jnp.inf, jnp.float32)
        )

        def value_step(j, carry):
            total, acc = carry
            block = ids_ref[tile * MAXB + j]
            w = jnp.exp(s_ref[j] - high)
            total = total + jnp.sum(w, axis=0, keepdims=True)
            acc = acc + jnp.dot(
                vt_ref[block, rows, :], w.astype(jnp.bfloat16), preferred_element_type=jnp.float32
            )
            return total, acc

        total, acc = lax.fori_loop(
            0,
            used,
            value_step,
            (jnp.zeros((1, wide), jnp.float32), jnp.zeros((LANES, wide), jnp.float32)),
        )
        o_ref[0, pl.ds(pair * LANES, HD), :] = (acc[:HD, :LANES] / total[:, :LANES]).astype(
            jnp.bfloat16
        )
        o_ref[0, pl.ds(pair * LANES + HD, HD), :] = (
            acc[HD:, LANES:] / total[:, LANES:]
        ).astype(jnp.bfloat16)


def attend(local_ids, tile_blocks, counts, queries_t, keys, values_t):
    tiles = queries_t.shape[0]
    near = keys.shape[0]
    grid_spec = pltpu.PrefetchScalarGridSpec(
        num_scalar_prefetch=3,
        grid=(tiles,),
        in_specs=[
            pl.BlockSpec((1, D, CELLS), lambda t, *_: (t, 0, 0)),
            pl.BlockSpec((near, OBS, D), lambda t, *_: (0, 0, 0)),
            pl.BlockSpec((near, D, OBS), lambda t, *_: (0, 0, 0)),
        ],
        out_specs=pl.BlockSpec((1, D, CELLS), lambda t, *_: (t, 0, 0)),
        scratch_shapes=[pltpu.VMEM((MAXB, OBS, 2 * LANES), jnp.float32)],
    )
    return pl.pallas_call(
        attend_kernel,
        grid_spec=grid_spec,
        out_shape=jax.ShapeDtypeStruct(queries_t.shape, jnp.bfloat16),
        compiler_params=pltpu.CompilerParams(vmem_limit_bytes=48 * 1024 * 1024),
    )(local_ids.reshape(-1), tile_blocks, counts, queries_t, keys, values_t)


def body(
    latent,
    query_gain,
    key_gain,
    output_gain,
    output_weight,
    observations,
    panels,
    instrument,
    observed_count,
    footprint,
    tile_blocks,
):
    block_count = observations.shape[0]
    position = lax.axis_index("lat")
    first_block = (position - 1) * block_count
    all_blocks = instrument.shape[0]
    table = lax.all_gather(panels, "lat", axis=0, tiled=True)
    kinds = table.shape[0] // CH
    near_obs = padded(observations, "lat", block_count)
    near_count = near_obs.shape[0]
    near_ids = jnp.clip(first_block + jnp.arange(near_count, dtype=jnp.int32), 0, all_blocks - 1)
    near_kinds = instrument[near_ids]
    counts = observed_count[near_ids]
    near_panels = table.reshape(kinds, CH, D)[near_kinds]
    embedded = jnp.einsum(
        "boc,bcd->bod", near_obs, near_panels, preferred_element_type=jnp.float32
    ).astype(jnp.bfloat16)
    keys = normalize(embedded, key_gain).astype(jnp.bfloat16)
    tiles = latent.shape[0] // CELLS
    queries = (latent.astype(jnp.float32) * query_gain).astype(jnp.bfloat16)
    queries_t = jnp.swapaxes(queries.reshape(tiles, CELLS, D), 1, 2)
    local_ids = (footprint - first_block).astype(jnp.int32)
    attended_t = attend(
        local_ids, tile_blocks.astype(jnp.int32), counts, queries_t, keys, jnp.swapaxes(embedded, 1, 2)
    )
    projected = jnp.einsum(
        "tdq,de->tqe", attended_t, output_weight, preferred_element_type=jnp.float32
    ).reshape(tiles * CELLS, D)
    mixed = latent.astype(jnp.float32) + projected
    return normalize(mixed, output_gain).astype(jnp.bfloat16)


def solution(mesh):
    return jax.shard_map(
        body,
        mesh=mesh,
        in_specs=(
            P(("groups", "lat"), None),
            P(),
            P(),
            P(),
            P(),
            P(("groups", "lat"), None, None),
            P("lat", None),
            P("groups"),
            P("groups"),
            P(("groups", "lat"), None),
            P(("groups", "lat")),
        ),
        out_specs=P(("groups", "lat"), None),
        check_vma=False,
    )
```

```python
import functools
import math

import jax
import jax.numpy as jnp
from jax import lax
from jax.experimental import pallas as pl
from jax.experimental.pallas import tpu as pltpu
from jax.sharding import PartitionSpec as P

D = 1536
HD = 64
CH = 128
CELLS = 128
OBS = 128
MAXB = 6
LANES = 128


def padded(value, axis, width):
    peers, length = lax.axis_size(axis), value.shape[0]
    up = [(i, i + 1) for i in range(peers - 1)]
    down = [(j, i) for i, j in up]
    before = lax.ppermute(value[length - width:], axis, up)
    after = lax.ppermute(value[:width], axis, down)
    return jnp.concatenate([before, value, after], axis=0)


def normalize(values, gain):
    values = values.astype(jnp.float32)
    return values * lax.rsqrt(jnp.mean(values * values, axis=-1, keepdims=True) + 1e-06) * gain


def attend_kernel(ids_ref, nb_ref, cnt_ref, qt_ref, k_ref, vt_ref, o_ref, s_ref):
    tile = pl.program_id(0)
    used = nb_ref[tile]
    scale = 1.0 / math.sqrt(HD)
    row = lax.broadcasted_iota(jnp.int32, (LANES, 1), 0)
    low = row < HD
    wide = 2 * LANES
    for pair in range(D // LANES):
        rows = pl.ds(pair * LANES, LANES)
        qt = qt_ref[0, rows, :].astype(jnp.float32)
        q2 = jnp.concatenate(
            [jnp.where(low, qt, 0.0), jnp.where(low, 0.0, qt)], axis=1
        ).astype(jnp.bfloat16)

        high = jnp.full((1, wide), -jnp.inf, jnp.float32)
        for j in range(MAXB):
            block = ids_ref[tile * MAXB + j]
            keys = k_ref[block, :, rows]
            s = jnp.dot(keys, q2, preferred_element_type=jnp.float32) * scale
            s = jnp.where((row < cnt_ref[block]) & (j < used), s, -jnp.inf)
            s_ref[j] = s
            high = jnp.maximum(high, jnp.max(s, axis=0, keepdims=True))
        total = jnp.zeros((1, wide), jnp.float32)
        acc = jnp.zeros((LANES, wide), jnp.float32)
        for j in range(MAXB):
            block = ids_ref[tile * MAXB + j]
            w = jnp.exp(s_ref[j] - high)
            total = total + jnp.sum(w, axis=0, keepdims=True)
            acc = acc + jnp.dot(
                vt_ref[block, rows, :], w.astype(jnp.bfloat16), preferred_element_type=jnp.float32
            )
        o_ref[0, pl.ds(pair * LANES, HD), :] = (acc[:HD, :LANES] / total[:, :LANES]).astype(
            jnp.bfloat16
        )
        o_ref[0, pl.ds(pair * LANES + HD, HD), :] = (
            acc[HD:, LANES:] / total[:, LANES:]
        ).astype(jnp.bfloat16)


def attend(local_ids, tile_blocks, counts, queries_t, keys, values_t):
    tiles = queries_t.shape[0]
    near = keys.shape[0]
    grid_spec = pltpu.PrefetchScalarGridSpec(
        num_scalar_prefetch=3,
        grid=(tiles,),
        in_specs=[
            pl.BlockSpec((1, D, CELLS), lambda t, *_: (t, 0, 0)),
            pl.BlockSpec((near, OBS, D), lambda t, *_: (0, 0, 0)),
            pl.BlockSpec((near, D, OBS), lambda t, *_: (0, 0, 0)),
        ],
        out_specs=pl.BlockSpec((1, D, CELLS), lambda t, *_: (t, 0, 0)),
        scratch_shapes=[pltpu.VMEM((MAXB, OBS, 2 * LANES), jnp.float32)],
    )
    return pl.pallas_call(
        attend_kernel,
        grid_spec=grid_spec,
        out_shape=jax.ShapeDtypeStruct(queries_t.shape, jnp.bfloat16),
        compiler_params=pltpu.CompilerParams(vmem_limit_bytes=48 * 1024 * 1024),
    )(local_ids.reshape(-1), tile_blocks, counts, queries_t, keys, values_t)


def body(
    latent,
    query_gain,
    key_gain,
    output_gain,
    output_weight,
    observations,
    panels,
    instrument,
    observed_count,
    footprint,
    tile_blocks,
):
    block_count = observations.shape[0]
    position = lax.axis_index("lat")
    first_block = (position - 1) * block_count
    all_blocks = instrument.shape[0]
    table = lax.all_gather(panels, "lat", axis=0, tiled=True)
    kinds = table.shape[0] // CH
    near_obs = padded(observations, "lat", block_count)
    near_count = near_obs.shape[0]
    near_ids = jnp.clip(first_block + jnp.arange(near_count, dtype=jnp.int32), 0, all_blocks - 1)
    near_kinds = instrument[near_ids]
    counts = observed_count[near_ids]
    near_panels = table.reshape(kinds, CH, D)[near_kinds]
    embedded = jnp.einsum(
        "boc,bcd->bod", near_obs, near_panels, preferred_element_type=jnp.float32
    ).astype(jnp.bfloat16)
    keys = normalize(embedded, key_gain).astype(jnp.bfloat16)
    tiles = latent.shape[0] // CELLS
    queries = (latent.astype(jnp.float32) * query_gain).astype(jnp.bfloat16)
    queries_t = jnp.swapaxes(queries.reshape(tiles, CELLS, D), 1, 2)
    local_ids = jnp.clip(footprint - first_block, 0, near_count - 1).astype(jnp.int32)
    attended_t = attend(
        local_ids, tile_blocks.astype(jnp.int32), counts, queries_t, keys, jnp.swapaxes(embedded, 1, 2)
    )
    projected = jnp.einsum(
        "tdq,de->tqe", attended_t, output_weight, preferred_element_type=jnp.float32
    ).reshape(tiles * CELLS, D)
    mixed = latent.astype(jnp.float32) + projected
    return normalize(mixed, output_gain).astype(jnp.bfloat16)


def solution(mesh):
    return jax.shard_map(
        body,
        mesh=mesh,
        in_specs=(
            P(("groups", "lat"), None),
            P(),
            P(),
            P(),
            P(),
            P(("groups", "lat"), None, None),
            P("lat", None),
            P("groups"),
            P("groups"),
            P(("groups", "lat"), None),
            P(("groups", "lat")),
        ),
        out_specs=P(("groups", "lat"), None),
        check_vma=False,
    )
```

```python
import functools
import math

import jax
import jax.numpy as jnp
from jax import lax
from jax.experimental import pallas as pl
from jax.experimental.pallas import tpu as pltpu
from jax.sharding import PartitionSpec as P

D = 1536
HD = 64
CH = 128
CELLS = 128
OBS = 128
MAXB = 6
LANES = 128


def padded(value, axis, width):
    peers, length = lax.axis_size(axis), value.shape[0]
    up = [(i, i + 1) for i in range(peers - 1)]
    down = [(j, i) for i, j in up]
    before = lax.ppermute(value[length - width:], axis, up)
    after = lax.ppermute(value[:width], axis, down)
    return jnp.concatenate([before, value, after], axis=0)


def normalize(values, gain):
    values = values.astype(jnp.float32)
    return values * lax.rsqrt(jnp.mean(values * values, axis=-1, keepdims=True) + 1e-06) * gain


def attend_kernel(ids_ref, nb_ref, cnt_ref, qt_ref, k_ref, vt_ref, o_ref, s_ref):
    tile = pl.program_id(0)
    used = nb_ref[tile]
    scale = 1.0 / math.sqrt(HD)
    row = lax.broadcasted_iota(jnp.int32, (LANES, 1), 0)
    low = row < HD
    wide = 2 * LANES
    for pair in range(D // LANES):
        rows = pl.ds(pair * LANES, LANES)
        qt = qt_ref[0, rows, :].astype(jnp.float32)
        q2 = jnp.concatenate(
            [jnp.where(low, qt, 0.0), jnp.where(low, 0.0, qt)], axis=1
        ).astype(jnp.bfloat16)

        high = jnp.full((1, wide), -jnp.inf, jnp.float32)
        for j in range(MAXB):
            block = ids_ref[tile * MAXB + j]
            keys = k_ref[block, :, rows]
            s = jnp.dot(keys, q2, preferred_element_type=jnp.float32) * scale
            s = jnp.where((row < cnt_ref[block]) & (j < used), s, -jnp.inf)
            s_ref[j] = s
            high = jnp.maximum(high, jnp.max(s, axis=0, keepdims=True))
        total = jnp.zeros((1, wide), jnp.float32)
        acc = jnp.zeros((LANES, wide), jnp.float32)
        for j in range(MAXB):
            block = ids_ref[tile * MAXB + j]
            w = jnp.exp(s_ref[j] - high)
            total = total + jnp.sum(w, axis=0, keepdims=True)
            acc = acc + jnp.dot(
                vt_ref[block, rows, :], w.astype(jnp.bfloat16), preferred_element_type=jnp.float32
            )
        o_ref[0, pl.ds(pair * LANES, HD), :] = (acc[:HD, :LANES] / total[:, :LANES]).astype(
            jnp.bfloat16
        )
        o_ref[0, pl.ds(pair * LANES + HD, HD), :] = (
            acc[HD:, LANES:] / total[:, LANES:]
        ).astype(jnp.bfloat16)


def embed_kernel(kinds_ref, obs_ref, panel_ref, gain_ref, k_ref, vt_ref):
    embedded = jnp.dot(obs_ref[0], panel_ref[...], preferred_element_type=jnp.float32)
    embedded = embedded.astype(jnp.bfloat16).astype(jnp.float32)
    scale = lax.rsqrt(jnp.mean(embedded * embedded, axis=1, keepdims=True) + 1e-06)
    k_ref[0] = (embedded * scale * gain_ref[...]).astype(jnp.bfloat16)
    vt_ref[0] = embedded.T.astype(jnp.bfloat16)


def embed(kinds, near_obs, table, key_gain):
    near = near_obs.shape[0]
    grid_spec = pltpu.PrefetchScalarGridSpec(
        num_scalar_prefetch=1,
        grid=(near,),
        in_specs=[
            pl.BlockSpec((1, OBS, CH), lambda b, kinds: (b, 0, 0)),
            pl.BlockSpec((CH, D), lambda b, kinds: (kinds[b], 0)),
            pl.BlockSpec((1, D), lambda b, kinds: (0, 0)),
        ],
        out_specs=[
            pl.BlockSpec((1, OBS, D), lambda b, kinds: (b, 0, 0)),
            pl.BlockSpec((1, D, OBS), lambda b, kinds: (b, 0, 0)),
        ],
    )
    return pl.pallas_call(
        embed_kernel,
        grid_spec=grid_spec,
        out_shape=[
            jax.ShapeDtypeStruct((near, OBS, D), jnp.bfloat16),
            jax.ShapeDtypeStruct((near, D, OBS), jnp.bfloat16),
        ],
    )(kinds, near_obs, table, key_gain.reshape(1, D))


def attend(local_ids, tile_blocks, counts, queries_t, keys, values_t):
    tiles = queries_t.shape[0]
    near = keys.shape[0]
    grid_spec = pltpu.PrefetchScalarGridSpec(
        num_scalar_prefetch=3,
        grid=(tiles,),
        in_specs=[
            pl.BlockSpec((1, D, CELLS), lambda t, *_: (t, 0, 0)),
            pl.BlockSpec((near, OBS, D), lambda t, *_: (0, 0, 0)),
            pl.BlockSpec((near, D, OBS), lambda t, *_: (0, 0, 0)),
        ],
        out_specs=pl.BlockSpec((1, D, CELLS), lambda t, *_: (t, 0, 0)),
        scratch_shapes=[pltpu.VMEM((MAXB, OBS, 2 * LANES), jnp.float32)],
    )
    return pl.pallas_call(
        attend_kernel,
        grid_spec=grid_spec,
        out_shape=jax.ShapeDtypeStruct(queries_t.shape, jnp.bfloat16),
        compiler_params=pltpu.CompilerParams(vmem_limit_bytes=48 * 1024 * 1024),
    )(local_ids.reshape(-1), tile_blocks, counts, queries_t, keys, values_t)


def body(
    latent,
    query_gain,
    key_gain,
    output_gain,
    output_weight,
    observations,
    panels,
    instrument,
    observed_count,
    footprint,
    tile_blocks,
):
    block_count = observations.shape[0]
    position = lax.axis_index("lat")
    first_block = (position - 1) * block_count
    all_blocks = instrument.shape[0]
    table = lax.all_gather(panels, "lat", axis=0, tiled=True)
    kinds = table.shape[0] // CH
    near_obs = padded(observations, "lat", block_count)
    near_count = near_obs.shape[0]
    near_ids = jnp.clip(first_block + jnp.arange(near_count, dtype=jnp.int32), 0, all_blocks - 1)
    near_kinds = instrument[near_ids]
    counts = observed_count[near_ids]
    near_kinds = jnp.clip(near_kinds, 0, kinds - 1).astype(jnp.int32)
    keys, values_t = embed(near_kinds, near_obs, table, key_gain.astype(jnp.float32))
    tiles = latent.shape[0] // CELLS
    queries = (latent.astype(jnp.float32) * query_gain).astype(jnp.bfloat16)
    queries_t = jnp.swapaxes(queries.reshape(tiles, CELLS, D), 1, 2)
    local_ids = jnp.clip(footprint - first_block, 0, near_count - 1).astype(jnp.int32)
    attended_t = attend(
        local_ids, tile_blocks.astype(jnp.int32), counts, queries_t, keys, values_t
    )
    projected = jnp.einsum(
        "tdq,de->tqe", attended_t, output_weight, preferred_element_type=jnp.float32
    ).reshape(tiles * CELLS, D)
    mixed = latent.astype(jnp.float32) + projected
    return normalize(mixed, output_gain).astype(jnp.bfloat16)


def solution(mesh):
    return jax.shard_map(
        body,
        mesh=mesh,
        in_specs=(
            P(("groups", "lat"), None),
            P(),
            P(),
            P(),
            P(),
            P(("groups", "lat"), None, None),
            P("lat", None),
            P("groups"),
            P("groups"),
            P(("groups", "lat"), None),
            P(("groups", "lat")),
        ),
        out_specs=P(("groups", "lat"), None),
        check_vma=False,
    )
```

```python
import functools
import math

import jax
import jax.numpy as jnp
from jax import lax
from jax.experimental import pallas as pl
from jax.experimental.pallas import tpu as pltpu
from jax.sharding import PartitionSpec as P

D = 1536
HD = 64
CH = 128
CELLS = 128
OBS = 128
MAXB = 6
LANES = 128


def padded(value, axis, width):
    peers, length = lax.axis_size(axis), value.shape[0]
    up = [(i, i + 1) for i in range(peers - 1)]
    down = [(j, i) for i, j in up]
    before = lax.ppermute(value[length - width:], axis, up)
    after = lax.ppermute(value[:width], axis, down)
    return jnp.concatenate([before, value, after], axis=0)


def normalize(values, gain):
    values = values.astype(jnp.float32)
    return values * lax.rsqrt(jnp.mean(values * values, axis=-1, keepdims=True) + 1e-06) * gain


def attend_kernel(ids_ref, nb_ref, cnt_ref, qt_ref, k_ref, v_ref, o_ref, s_ref):
    tile = pl.program_id(0)
    used = nb_ref[tile]
    scale = 1.0 / math.sqrt(HD)
    row = lax.broadcasted_iota(jnp.int32, (LANES, 1), 0)
    low = row < HD
    wide = 2 * LANES
    for pair in range(D // LANES):
        rows = pl.ds(pair * LANES, LANES)
        qt = qt_ref[0, rows, :].astype(jnp.float32)
        q2 = jnp.concatenate(
            [jnp.where(low, qt, 0.0), jnp.where(low, 0.0, qt)], axis=1
        ).astype(jnp.bfloat16)

        high = jnp.full((1, wide), -jnp.inf, jnp.float32)
        for j in range(MAXB):
            block = ids_ref[tile * MAXB + j]
            keys = k_ref[block, :, rows]
            s = jnp.dot(keys, q2, preferred_element_type=jnp.float32) * scale
            s = jnp.where((row < cnt_ref[block]) & (j < used), s, -jnp.inf)
            s_ref[j] = s
            high = jnp.maximum(high, jnp.max(s, axis=0, keepdims=True))
        total = jnp.zeros((1, wide), jnp.float32)
        acc = jnp.zeros((wide, LANES), jnp.float32)
        for j in range(MAXB):
            block = ids_ref[tile * MAXB + j]
            w = jnp.exp(s_ref[j] - high)
            total = total + jnp.sum(w, axis=0, keepdims=True)
            acc = acc + lax.dot_general(
                w.astype(jnp.bfloat16),
                v_ref[block, :, rows],
                (((0,), (0,)), ((), ())),
                preferred_element_type=jnp.float32,
            )
        total = jnp.broadcast_to(total, (8, wide)).T[:, :1]
        lane = lax.broadcasted_iota(jnp.int32, (1, LANES), 1)
        out = jnp.where(
            lane < HD, acc[:LANES] / total[:LANES], acc[LANES:] / total[LANES:]
        )
        o_ref[:, rows] = out.astype(jnp.bfloat16)


def embed_kernel(kinds_ref, obs_ref, panel_ref, gain_ref, k_ref, vt_ref):
    embedded = jnp.dot(obs_ref[0], panel_ref[...], preferred_element_type=jnp.float32)
    embedded = embedded.astype(jnp.bfloat16).astype(jnp.float32)
    scale = lax.rsqrt(jnp.mean(embedded * embedded, axis=1, keepdims=True) + 1e-06)
    k_ref[0] = (embedded * scale * gain_ref[...]).astype(jnp.bfloat16)
    vt_ref[0] = embedded.astype(jnp.bfloat16)


def embed(kinds, near_obs, table, key_gain):
    near = near_obs.shape[0]
    grid_spec = pltpu.PrefetchScalarGridSpec(
        num_scalar_prefetch=1,
        grid=(near,),
        in_specs=[
            pl.BlockSpec((1, OBS, CH), lambda b, kinds: (b, 0, 0)),
            pl.BlockSpec((CH, D), lambda b, kinds: (kinds[b], 0)),
            pl.BlockSpec((1, D), lambda b, kinds: (0, 0)),
        ],
        out_specs=[
            pl.BlockSpec((1, OBS, D), lambda b, kinds: (b, 0, 0)),
            pl.BlockSpec((1, OBS, D), lambda b, kinds: (b, 0, 0)),
        ],
    )
    return pl.pallas_call(
        embed_kernel,
        grid_spec=grid_spec,
        out_shape=[
            jax.ShapeDtypeStruct((near, OBS, D), jnp.bfloat16),
            jax.ShapeDtypeStruct((near, OBS, D), jnp.bfloat16),
        ],
    )(kinds, near_obs, table, key_gain.reshape(1, D))


def attend(local_ids, tile_blocks, counts, queries_t, keys, values):
    tiles = queries_t.shape[0]
    near = keys.shape[0]
    grid_spec = pltpu.PrefetchScalarGridSpec(
        num_scalar_prefetch=3,
        grid=(tiles,),
        in_specs=[
            pl.BlockSpec((1, D, CELLS), lambda t, *_: (t, 0, 0)),
            pl.BlockSpec((near, OBS, D), lambda t, *_: (0, 0, 0)),
            pl.BlockSpec((near, OBS, D), lambda t, *_: (0, 0, 0)),
        ],
        out_specs=pl.BlockSpec((CELLS, D), lambda t, *_: (t, 0)),
        scratch_shapes=[pltpu.VMEM((MAXB, OBS, 2 * LANES), jnp.float32)],
    )
    return pl.pallas_call(
        attend_kernel,
        grid_spec=grid_spec,
        out_shape=jax.ShapeDtypeStruct((tiles * CELLS, D), jnp.bfloat16),
        compiler_params=pltpu.CompilerParams(vmem_limit_bytes=48 * 1024 * 1024),
    )(local_ids.reshape(-1), tile_blocks, counts, queries_t, keys, values)


def body(
    latent,
    query_gain,
    key_gain,
    output_gain,
    output_weight,
    observations,
    panels,
    instrument,
    observed_count,
    footprint,
    tile_blocks,
):
    block_count = observations.shape[0]
    position = lax.axis_index("lat")
    first_block = (position - 1) * block_count
    all_blocks = instrument.shape[0]
    table = lax.all_gather(panels, "lat", axis=0, tiled=True)
    kinds = table.shape[0] // CH
    near_obs = padded(observations, "lat", block_count)
    near_count = near_obs.shape[0]
    near_ids = jnp.clip(first_block + jnp.arange(near_count, dtype=jnp.int32), 0, all_blocks - 1)
    near_kinds = instrument[near_ids]
    counts = observed_count[near_ids]
    near_kinds = jnp.clip(near_kinds, 0, kinds - 1).astype(jnp.int32)
    keys, values = embed(near_kinds, near_obs, table, key_gain.astype(jnp.float32))
    tiles = latent.shape[0] // CELLS
    queries = (latent.astype(jnp.float32) * query_gain).astype(jnp.bfloat16)
    queries_t = jnp.swapaxes(queries.reshape(tiles, CELLS, D), 1, 2)
    local_ids = jnp.clip(footprint - first_block, 0, near_count - 1).astype(jnp.int32)
    attended = attend(local_ids, tile_blocks.astype(jnp.int32), counts, queries_t, keys, values)
    mixed = latent.astype(jnp.float32) + jnp.dot(
        attended, output_weight, preferred_element_type=jnp.float32
    )
    return normalize(mixed, output_gain).astype(jnp.bfloat16)


def solution(mesh):
    return jax.shard_map(
        body,
        mesh=mesh,
        in_specs=(
            P(("groups", "lat"), None),
            P(),
            P(),
            P(),
            P(),
            P(("groups", "lat"), None, None),
            P("lat", None),
            P("groups"),
            P("groups"),
            P(("groups", "lat"), None),
            P(("groups", "lat")),
        ),
        out_specs=P(("groups", "lat"), None),
        check_vma=False,
    )
```

```python
import functools
import math

import jax
import jax.numpy as jnp
from jax import lax
from jax.experimental import pallas as pl
from jax.experimental.pallas import tpu as pltpu
from jax.sharding import PartitionSpec as P

D = 1536
HD = 64
CH = 128
CELLS = 128
OBS = 128
MAXB = 6
LANES = 128


def padded(value, axis, width):
    peers, length = lax.axis_size(axis), value.shape[0]
    up = [(i, i + 1) for i in range(peers - 1)]
    down = [(j, i) for i, j in up]
    before = lax.ppermute(value[length - width:], axis, up)
    after = lax.ppermute(value[:width], axis, down)
    return jnp.concatenate([before, value, after], axis=0)


def normalize(values, gain):
    values = values.astype(jnp.float32)
    return values * lax.rsqrt(jnp.mean(values * values, axis=-1, keepdims=True) + 1e-06) * gain


def attend_kernel(ids_ref, nb_ref, cnt_ref, qt_ref, k_ref, vt_ref, o_ref, s_ref):
    tile = pl.program_id(0)
    used = nb_ref[tile]
    scale = 1.0 / math.sqrt(HD)
    row = lax.broadcasted_iota(jnp.int32, (LANES, 1), 0)
    low = row < HD
    wide = 2 * LANES
    for pair in range(D // LANES):
        rows = pl.ds(pair * LANES, LANES)
        qt = qt_ref[0, rows, :].astype(jnp.float32)
        q2 = jnp.concatenate(
            [jnp.where(low, qt, 0.0), jnp.where(low, 0.0, qt)], axis=1
        ).astype(jnp.bfloat16)

        high = jnp.full((1, wide), -jnp.inf, jnp.float32)
        for j in range(MAXB):
            block = ids_ref[tile * MAXB + j]
            keys = k_ref[block, :, rows]
            s = jnp.dot(keys, q2, preferred_element_type=jnp.float32) * scale
            s = jnp.where((row < cnt_ref[block]) & (j < used), s, -jnp.inf)
            s_ref[j] = s
            high = jnp.maximum(high, jnp.max(s, axis=0, keepdims=True))
        total = jnp.zeros((1, wide), jnp.float32)
        acc = jnp.zeros((LANES, wide), jnp.float32)
        for j in range(MAXB):
            block = ids_ref[tile * MAXB + j]
            w = jnp.exp(s_ref[j] - high)
            total = total + jnp.sum(w, axis=0, keepdims=True)
            acc = acc + jnp.dot(
                vt_ref[block, rows, :], w.astype(jnp.bfloat16), preferred_element_type=jnp.float32
            )
        o_ref[0, pl.ds(pair * LANES, HD), :] = (acc[:HD, :LANES] / total[:, :LANES]).astype(
            jnp.bfloat16
        )
        o_ref[0, pl.ds(pair * LANES + HD, HD), :] = (
            acc[HD:, LANES:] / total[:, LANES:]
        ).astype(jnp.bfloat16)


def attend_kernel(
    kinds_ref, ids_ref, nb_ref, cnt_ref, obs_ref, table_ref, gain_ref, qt_ref, o_ref,
    k_ref, vt_ref, s_ref,
):
    tile = pl.program_id(0)

    @pl.when(tile == 0)
    def _():
        for b in range(k_ref.shape[0]):
            start = pl.multiple_of(kinds_ref[b] * CH, CH)
            embedded = jnp.dot(
                obs_ref[b], table_ref[pl.ds(start, CH), :], preferred_element_type=jnp.float32
            )
            embedded = embedded.astype(jnp.bfloat16).astype(jnp.float32)
            norm = lax.rsqrt(jnp.mean(embedded * embedded, axis=1, keepdims=True) + 1e-06)
            k_ref[b] = (embedded * norm * gain_ref[...]).astype(jnp.bfloat16)
            vt_ref[b] = embedded.T.astype(jnp.bfloat16)

    used = nb_ref[tile]
    scale = 1.0 / math.sqrt(HD)
    row = lax.broadcasted_iota(jnp.int32, (LANES, 1), 0)
    low = row < HD
    wide = 2 * LANES
    for pair in range(D // LANES):
        rows = pl.ds(pair * LANES, LANES)
        qt = qt_ref[0, rows, :].astype(jnp.float32)
        q2 = jnp.concatenate(
            [jnp.where(low, qt, 0.0), jnp.where(low, 0.0, qt)], axis=1
        ).astype(jnp.bfloat16)
        high = jnp.full((1, wide), -jnp.inf, jnp.float32)
        for j in range(MAXB):
            block = ids_ref[tile * MAXB + j]
            keys = k_ref[block, :, rows]
            s = jnp.dot(keys, q2, preferred_element_type=jnp.float32) * scale
            s = jnp.where((row < cnt_ref[block]) & (j < used), s, -jnp.inf)
            s_ref[j] = s
            high = jnp.maximum(high, jnp.max(s, axis=0, keepdims=True))
        total = jnp.zeros((1, wide), jnp.float32)
        acc = jnp.zeros((LANES, wide), jnp.float32)
        for j in range(MAXB):
            block = ids_ref[tile * MAXB + j]
            w = jnp.exp(s_ref[j] - high)
            total = total + jnp.sum(w, axis=0, keepdims=True)
            acc = acc + jnp.dot(
                vt_ref[block, rows, :], w.astype(jnp.bfloat16), preferred_element_type=jnp.float32
            )
        o_ref[0, pl.ds(pair * LANES, HD), :] = (acc[:HD, :LANES] / total[:, :LANES]).astype(
            jnp.bfloat16
        )
        o_ref[0, pl.ds(pair * LANES + HD, HD), :] = (
            acc[HD:, LANES:] / total[:, LANES:]
        ).astype(jnp.bfloat16)


def attend(kinds, local_ids, tile_blocks, counts, near_obs, table, key_gain, queries_t):
    tiles = queries_t.shape[0]
    near = near_obs.shape[0]
    grid_spec = pltpu.PrefetchScalarGridSpec(
        num_scalar_prefetch=4,
        grid=(tiles,),
        in_specs=[
            pl.BlockSpec(near_obs.shape, lambda t, *_: (0, 0, 0)),
            pl.BlockSpec(table.shape, lambda t, *_: (0, 0)),
            pl.BlockSpec((1, D), lambda t, *_: (0, 0)),
            pl.BlockSpec((1, D, CELLS), lambda t, *_: (t, 0, 0)),
        ],
        out_specs=pl.BlockSpec((1, D, CELLS), lambda t, *_: (t, 0, 0)),
        scratch_shapes=[
            pltpu.VMEM((near, OBS, D), jnp.bfloat16),
            pltpu.VMEM((near, D, OBS), jnp.bfloat16),
            pltpu.VMEM((MAXB, OBS, 2 * LANES), jnp.float32),
        ],
    )
    return pl.pallas_call(
        attend_kernel,
        grid_spec=grid_spec,
        out_shape=jax.ShapeDtypeStruct(queries_t.shape, jnp.bfloat16),
        compiler_params=pltpu.CompilerParams(
            dimension_semantics=("arbitrary",), vmem_limit_bytes=48 * 1024 * 1024
        ),
    )(kinds, local_ids.reshape(-1), tile_blocks, counts, near_obs, table, key_gain.reshape(1, D), queries_t)


def body(
    latent,
    query_gain,
    key_gain,
    output_gain,
    output_weight,
    observations,
    panels,
    instrument,
    observed_count,
    footprint,
    tile_blocks,
):
    block_count = observations.shape[0]
    position = lax.axis_index("lat")
    first_block = (position - 1) * block_count
    all_blocks = instrument.shape[0]
    table = lax.all_gather(panels, "lat", axis=0, tiled=True)
    kinds = table.shape[0] // CH
    near_obs = padded(observations, "lat", block_count)
    near_count = near_obs.shape[0]
    near_ids = jnp.clip(first_block + jnp.arange(near_count, dtype=jnp.int32), 0, all_blocks - 1)
    near_kinds = instrument[near_ids]
    counts = observed_count[near_ids]
    near_kinds = jnp.clip(near_kinds, 0, kinds - 1).astype(jnp.int32)
    tiles = latent.shape[0] // CELLS
    queries = (latent.astype(jnp.float32) * query_gain).astype(jnp.bfloat16)
    queries_t = jnp.swapaxes(queries.reshape(tiles, CELLS, D), 1, 2)
    local_ids = jnp.clip(footprint - first_block, 0, near_count - 1).astype(jnp.int32)
    attended_t = attend(
        near_kinds,
        local_ids,
        tile_blocks.astype(jnp.int32),
        counts,
        near_obs,
        table,
        key_gain.astype(jnp.float32),
        queries_t,
    )
    projected = jnp.einsum(
        "tdq,de->tqe", attended_t, output_weight, preferred_element_type=jnp.float32
    ).reshape(tiles * CELLS, D)
    mixed = latent.astype(jnp.float32) + projected
    return normalize(mixed, output_gain).astype(jnp.bfloat16)


def solution(mesh):
    return jax.shard_map(
        body,
        mesh=mesh,
        in_specs=(
            P(("groups", "lat"), None),
            P(),
            P(),
            P(),
            P(),
            P(("groups", "lat"), None, None),
            P("lat", None),
            P("groups"),
            P("groups"),
            P(("groups", "lat"), None),
            P(("groups", "lat")),
        ),
        out_specs=P(("groups", "lat"), None),
        check_vma=False,
    )
```

```python
import functools
import math

import jax
import jax.numpy as jnp
from jax import lax
from jax.experimental import pallas as pl
from jax.experimental.pallas import tpu as pltpu
from jax.sharding import PartitionSpec as P

D = 1536
HD = 64
CH = 128
CELLS = 128
OBS = 128
MAXB = 6
LANES = 128


def padded(value, axis, width):
    peers, length = lax.axis_size(axis), value.shape[0]
    up = [(i, i + 1) for i in range(peers - 1)]
    down = [(j, i) for i, j in up]
    before = lax.ppermute(value[length - width:], axis, up)
    after = lax.ppermute(value[:width], axis, down)
    return jnp.concatenate([before, value, after], axis=0)


def normalize(values, gain):
    values = values.astype(jnp.float32)
    return values * lax.rsqrt(jnp.mean(values * values, axis=-1, keepdims=True) + 1e-06) * gain


def attend_kernel(
    kinds_ref, ids_ref, nb_ref, cnt_ref, obs_ref, table_ref, gain_ref, qt_ref, o_ref,
    k_ref, vt_ref, s_ref,
):
    tile = pl.program_id(0)

    @pl.when(tile == 0)
    def _():
        for b in range(k_ref.shape[0]):
            start = pl.multiple_of(kinds_ref[b] * CH, CH)
            embedded = jnp.dot(
                obs_ref[b], table_ref[pl.ds(start, CH), :], preferred_element_type=jnp.float32
            )
            embedded = embedded.astype(jnp.bfloat16).astype(jnp.float32)
            norm = lax.rsqrt(jnp.mean(embedded * embedded, axis=1, keepdims=True) + 1e-06)
            k_ref[b] = (embedded * norm * gain_ref[...]).astype(jnp.bfloat16)
            vt_ref[b] = embedded.T.astype(jnp.bfloat16)

    used = nb_ref[tile]
    scale = 1.0 / math.sqrt(HD)
    row = lax.broadcasted_iota(jnp.int32, (LANES, 1), 0)
    low = row < HD
    wide = 2 * LANES
    for pair in range(D // LANES):
        rows = pl.ds(pair * LANES, LANES)
        qt = qt_ref[0, rows, :].astype(jnp.float32) * scale
        q2 = jnp.concatenate(
            [jnp.where(low, qt, 0.0), jnp.where(low, 0.0, qt)], axis=1
        ).astype(jnp.bfloat16)
        high = jnp.full((1, wide), -jnp.inf, jnp.float32)
        for j in range(MAXB):
            block = ids_ref[tile * MAXB + j]
            keys = k_ref[block, :, rows]
            s = jnp.dot(keys, q2, preferred_element_type=jnp.float32)
            s = jnp.where((row < cnt_ref[block]) & (j < used), s, -jnp.inf)
            s_ref[j] = s
            high = jnp.maximum(high, jnp.max(s, axis=0, keepdims=True))
        total = jnp.zeros((1, wide), jnp.float32)
        acc = jnp.zeros((LANES, wide), jnp.float32)
        for j in range(0, MAXB, 2):
            ws, vs = [], []
            for i in (j, j + 1):
                w = jnp.exp(s_ref[i] - high)
                total = total + jnp.sum(w, axis=0, keepdims=True)
                ws.append(w.astype(jnp.bfloat16))
                vs.append(vt_ref[ids_ref[tile * MAXB + i], rows, :])
            acc = acc + jnp.dot(
                jnp.concatenate(vs, axis=1),
                jnp.concatenate(ws, axis=0),
                preferred_element_type=jnp.float32,
            )
        o_ref[0, pl.ds(pair * LANES, HD), :] = (acc[:HD, :LANES] / total[:, :LANES]).astype(
            jnp.bfloat16
        )
        o_ref[0, pl.ds(pair * LANES + HD, HD), :] = (
            acc[HD:, LANES:] / total[:, LANES:]
        ).astype(jnp.bfloat16)


def attend(kinds, local_ids, tile_blocks, counts, near_obs, table, key_gain, queries_t):
    tiles = queries_t.shape[0]
    near = near_obs.shape[0]
    grid_spec = pltpu.PrefetchScalarGridSpec(
        num_scalar_prefetch=4,
        grid=(tiles,),
        in_specs=[
            pl.BlockSpec(near_obs.shape, lambda t, *_: (0, 0, 0)),
            pl.BlockSpec(table.shape, lambda t, *_: (0, 0)),
            pl.BlockSpec((1, D), lambda t, *_: (0, 0)),
            pl.BlockSpec((1, D, CELLS), lambda t, *_: (t, 0, 0)),
        ],
        out_specs=pl.BlockSpec((1, D, CELLS), lambda t, *_: (t, 0, 0)),
        scratch_shapes=[
            pltpu.VMEM((near, OBS, D), jnp.bfloat16),
            pltpu.VMEM((near, D, OBS), jnp.bfloat16),
            pltpu.VMEM((MAXB, OBS, 2 * LANES), jnp.float32),
        ],
    )
    return pl.pallas_call(
        attend_kernel,
        grid_spec=grid_spec,
        out_shape=jax.ShapeDtypeStruct(queries_t.shape, jnp.bfloat16),
        compiler_params=pltpu.CompilerParams(
            dimension_semantics=("arbitrary",), vmem_limit_bytes=48 * 1024 * 1024
        ),
    )(kinds, local_ids.reshape(-1), tile_blocks, counts, near_obs, table, key_gain.reshape(1, D), queries_t)


def body(
    latent,
    query_gain,
    key_gain,
    output_gain,
    output_weight,
    observations,
    panels,
    instrument,
    observed_count,
    footprint,
    tile_blocks,
):
    block_count = observations.shape[0]
    position = lax.axis_index("lat")
    first_block = (position - 1) * block_count
    all_blocks = instrument.shape[0]
    table = lax.all_gather(panels, "lat", axis=0, tiled=True)
    kinds = table.shape[0] // CH
    near_obs = padded(observations, "lat", block_count)
    near_count = near_obs.shape[0]
    near_ids = jnp.clip(first_block + jnp.arange(near_count, dtype=jnp.int32), 0, all_blocks - 1)
    near_kinds = instrument[near_ids]
    counts = observed_count[near_ids]
    near_kinds = jnp.clip(near_kinds, 0, kinds - 1).astype(jnp.int32)
    tiles = latent.shape[0] // CELLS
    queries = (latent.astype(jnp.float32) * query_gain).astype(jnp.bfloat16)
    queries_t = jnp.swapaxes(queries.reshape(tiles, CELLS, D), 1, 2)
    local_ids = jnp.clip(footprint - first_block, 0, near_count - 1).astype(jnp.int32)
    attended_t = attend(
        near_kinds,
        local_ids,
        tile_blocks.astype(jnp.int32),
        counts,
        near_obs,
        table,
        key_gain.astype(jnp.float32),
        queries_t,
    )
    projected = jnp.einsum(
        "tdq,de->tqe", attended_t, output_weight, preferred_element_type=jnp.float32
    ).reshape(tiles * CELLS, D)
    mixed = latent.astype(jnp.float32) + projected
    return normalize(mixed, output_gain).astype(jnp.bfloat16)


def solution(mesh):
    return jax.shard_map(
        body,
        mesh=mesh,
        in_specs=(
            P(("groups", "lat"), None),
            P(),
            P(),
            P(),
            P(),
            P(("groups", "lat"), None, None),
            P("lat", None),
            P("groups"),
            P("groups"),
            P(("groups", "lat"), None),
            P(("groups", "lat")),
        ),
        out_specs=P(("groups", "lat"), None),
        check_vma=False,
    )
```

```python
import math

import jax
import jax.numpy as jnp
from jax import lax
from jax.experimental import pallas as pl
from jax.experimental.pallas import tpu as pltpu
from jax.sharding import PartitionSpec as P

D = 1536
HD = 64
CH = 128
CELLS = 128
OBS = 128
MAXB = 6
LANES = 128


def padded(value, axis, width):
    peers, length = lax.axis_size(axis), value.shape[0]
    up = [(i, i + 1) for i in range(peers - 1)]
    down = [(j, i) for i, j in up]
    before = lax.ppermute(value[length - width:], axis, up)
    after = lax.ppermute(value[:width], axis, down)
    return jnp.concatenate([before, value, after], axis=0)


def normalize(values, gain):
    values = values.astype(jnp.float32)
    return values * lax.rsqrt(jnp.mean(values * values, axis=-1, keepdims=True) + 1e-06) * gain


def attend_kernel(
    kinds_ref, ids_ref, nb_ref, cnt_ref, obs_ref, table_ref, gain_ref, qt_ref, o_ref,
    k_ref, vt_ref, s_ref, b_ref,
):
    tile = pl.program_id(0)

    @pl.when(tile == 0)
    def _():
        for b in range(k_ref.shape[0]):
            start = pl.multiple_of(kinds_ref[b] * CH, CH)
            embedded = jnp.dot(
                obs_ref[b], table_ref[pl.ds(start, CH), :], preferred_element_type=jnp.float32
            )
            embedded = embedded.astype(jnp.bfloat16).astype(jnp.float32)
            norm = lax.rsqrt(jnp.mean(embedded * embedded, axis=1, keepdims=True) + 1e-06)
            k_ref[b] = (embedded * norm * gain_ref[...]).astype(jnp.bfloat16)
            vt_ref[b] = embedded.T.astype(jnp.bfloat16)

    used = nb_ref[tile]
    scale = 1.0 / math.sqrt(HD)
    row = lax.broadcasted_iota(jnp.int32, (LANES, 1), 0)
    low = row < HD
    wide = 2 * LANES
    for j in range(MAXB):
        keep = (row < cnt_ref[ids_ref[tile * MAXB + j]]) & (j < used)
        b_ref[j] = jnp.broadcast_to(jnp.where(keep, 0.0, -jnp.inf), (OBS, wide))
    for pair in range(D // LANES):
        rows = pl.ds(pair * LANES, LANES)
        qt = qt_ref[0, rows, :].astype(jnp.float32) * scale
        q2 = jnp.concatenate(
            [jnp.where(low, qt, 0.0), jnp.where(low, 0.0, qt)], axis=1
        ).astype(jnp.bfloat16)
        high = jnp.full((1, wide), -jnp.inf, jnp.float32)
        for j in range(MAXB):
            block = ids_ref[tile * MAXB + j]
            keys = k_ref[block, :, rows]
            s = jnp.dot(keys, q2, preferred_element_type=jnp.float32) + b_ref[j]
            s_ref[j] = s
            high = jnp.maximum(high, jnp.max(s, axis=0, keepdims=True))
        total = jnp.zeros((1, wide), jnp.float32)
        acc = jnp.zeros((LANES, wide), jnp.float32)
        for j in range(MAXB):
            block = ids_ref[tile * MAXB + j]
            w = jnp.exp(s_ref[j] - high)
            total = total + jnp.sum(w, axis=0, keepdims=True)
            acc = acc + jnp.dot(
                vt_ref[block, rows, :], w.astype(jnp.bfloat16), preferred_element_type=jnp.float32
            )
        o_ref[0, pl.ds(pair * LANES, HD), :] = (acc[:HD, :LANES] / total[:, :LANES]).astype(
            jnp.bfloat16
        )
        o_ref[0, pl.ds(pair * LANES + HD, HD), :] = (
            acc[HD:, LANES:] / total[:, LANES:]
        ).astype(jnp.bfloat16)


def attend(kinds, local_ids, tile_blocks, counts, near_obs, table, key_gain, queries_t):
    tiles = queries_t.shape[0]
    near = near_obs.shape[0]
    grid_spec = pltpu.PrefetchScalarGridSpec(
        num_scalar_prefetch=4,
        grid=(tiles,),
        in_specs=[
            pl.BlockSpec(near_obs.shape, lambda t, *_: (0, 0, 0)),
            pl.BlockSpec(table.shape, lambda t, *_: (0, 0)),
            pl.BlockSpec((1, D), lambda t, *_: (0, 0)),
            pl.BlockSpec((1, D, CELLS), lambda t, *_: (t, 0, 0)),
        ],
        out_specs=pl.BlockSpec((1, D, CELLS), lambda t, *_: (t, 0, 0)),
        scratch_shapes=[
            pltpu.VMEM((near, OBS, D), jnp.bfloat16),
            pltpu.VMEM((near, D, OBS), jnp.bfloat16),
            pltpu.VMEM((MAXB, OBS, 2 * LANES), jnp.float32),
            pltpu.VMEM((MAXB, OBS, 2 * LANES), jnp.float32),
        ],
    )
    return pl.pallas_call(
        attend_kernel,
        grid_spec=grid_spec,
        out_shape=jax.ShapeDtypeStruct(queries_t.shape, jnp.bfloat16),
        compiler_params=pltpu.CompilerParams(
            dimension_semantics=("arbitrary",), vmem_limit_bytes=48 * 1024 * 1024
        ),
    )(kinds, local_ids.reshape(-1), tile_blocks, counts, near_obs, table, key_gain.reshape(1, D), queries_t)


def body(
    latent,
    query_gain,
    key_gain,
    output_gain,
    output_weight,
    observations,
    panels,
    instrument,
    observed_count,
    footprint,
    tile_blocks,
):
    block_count = observations.shape[0]
    position = lax.axis_index("lat")
    first_block = (position - 1) * block_count
    all_blocks = instrument.shape[0]
    table = lax.all_gather(panels, "lat", axis=0, tiled=True)
    kinds = table.shape[0] // CH
    near_obs = padded(observations, "lat", block_count)
    near_count = near_obs.shape[0]
    near_ids = jnp.clip(first_block + jnp.arange(near_count, dtype=jnp.int32), 0, all_blocks - 1)
    near_kinds = instrument[near_ids]
    counts = observed_count[near_ids]
    near_kinds = jnp.clip(near_kinds, 0, kinds - 1).astype(jnp.int32)
    tiles = latent.shape[0] // CELLS
    queries = (latent.astype(jnp.float32) * query_gain).astype(jnp.bfloat16)
    queries_t = jnp.swapaxes(queries.reshape(tiles, CELLS, D), 1, 2)
    local_ids = jnp.clip(footprint - first_block, 0, near_count - 1).astype(jnp.int32)
    attended_t = attend(
        near_kinds,
        local_ids,
        tile_blocks.astype(jnp.int32),
        counts,
        near_obs,
        table,
        key_gain.astype(jnp.float32),
        queries_t,
    )
    projected = jnp.einsum(
        "tdq,de->tqe", attended_t, output_weight, preferred_element_type=jnp.float32
    ).reshape(tiles * CELLS, D)
    mixed = latent.astype(jnp.float32) + projected
    return normalize(mixed, output_gain).astype(jnp.bfloat16)


def solution(mesh):
    return jax.shard_map(
        body,
        mesh=mesh,
        in_specs=(
            P(("groups", "lat"), None),
            P(),
            P(),
            P(),
            P(),
            P(("groups", "lat"), None, None),
            P("lat", None),
            P("groups"),
            P("groups"),
            P(("groups", "lat"), None),
            P(("groups", "lat")),
        ),
        out_specs=P(("groups", "lat"), None),
        check_vma=False,
    )
```

```python
import math

import jax
import jax.numpy as jnp
from jax import lax
from jax.experimental import pallas as pl
from jax.experimental.pallas import tpu as pltpu
from jax.sharding import PartitionSpec as P

D = 1536
HD = 64
CH = 128
CELLS = 128
OBS = 128
MAXB = 6
LANES = 128


def padded(value, axis, width):
    peers, length = lax.axis_size(axis), value.shape[0]
    up = [(i, i + 1) for i in range(peers - 1)]
    down = [(j, i) for i, j in up]
    before = lax.ppermute(value[length - width:], axis, up)
    after = lax.ppermute(value[:width], axis, down)
    return jnp.concatenate([before, value, after], axis=0)


def normalize(values, gain):
    values = values.astype(jnp.float32)
    return values * lax.rsqrt(jnp.mean(values * values, axis=-1, keepdims=True) + 1e-06) * gain


def finish(lat_ref, att, w_ref, ogain_ref, o_ref, tile):
    rows = pl.ds(pl.multiple_of(tile * CELLS, CELLS), CELLS)
    mixed = lat_ref[rows, :].astype(jnp.float32) + lax.dot_general(
        att, w_ref[...], (((0,), (0,)), ((), ())), preferred_element_type=jnp.float32
    )
    norm = lax.rsqrt(jnp.mean(mixed * mixed, axis=1, keepdims=True) + 1e-06)
    o_ref[rows, :] = (mixed * norm * ogain_ref[...]).astype(jnp.bfloat16)


def attend_kernel(
    kinds_ref, ids_ref, nb_ref, cnt_ref, obs_ref, table_ref, gain_ref, qt_ref, lat_ref,
    ogain_ref, w_hbm, o_ref, k_ref, vt_ref, s_ref, b_ref, att_ref, w_ref, sem,
):
    tile = pl.program_id(0)
    tiles = pl.num_programs(0)
    weight_copy = pltpu.make_async_copy(w_hbm, w_ref, sem)

    @pl.when(tile == 0)
    def _():
        weight_copy.start()
        att_ref[1] = jnp.zeros(att_ref.shape[1:], jnp.bfloat16)
        for b in range(k_ref.shape[0]):
            start = pl.multiple_of(kinds_ref[b] * CH, CH)
            embedded = jnp.dot(
                obs_ref[b], table_ref[pl.ds(start, CH), :], preferred_element_type=jnp.float32
            )
            embedded = embedded.astype(jnp.bfloat16).astype(jnp.float32)
            norm = lax.rsqrt(jnp.mean(embedded * embedded, axis=1, keepdims=True) + 1e-06)
            k_ref[b] = (embedded * norm * gain_ref[...]).astype(jnp.bfloat16)
            vt_ref[b] = embedded.T.astype(jnp.bfloat16)
        weight_copy.wait()

    slot = tile % 2
    finish(lat_ref, att_ref[1 - slot], w_ref, ogain_ref, o_ref, (tile + tiles - 1) % tiles)

    used = nb_ref[tile]
    scale = 1.0 / math.sqrt(HD)
    row = lax.broadcasted_iota(jnp.int32, (LANES, 1), 0)
    low = row < HD
    wide = 2 * LANES
    for j in range(MAXB):
        keep = (row < cnt_ref[ids_ref[tile * MAXB + j]]) & (j < used)
        b_ref[j] = jnp.broadcast_to(jnp.where(keep, 0.0, -jnp.inf), (OBS, wide))
    for pair in range(D // LANES):
        rows = pl.ds(pair * LANES, LANES)
        qt = qt_ref[0, rows, :].astype(jnp.float32) * scale
        q2 = jnp.concatenate(
            [jnp.where(low, qt, 0.0), jnp.where(low, 0.0, qt)], axis=1
        ).astype(jnp.bfloat16)
        high = jnp.full((1, wide), -jnp.inf, jnp.float32)
        for j in range(MAXB):
            block = ids_ref[tile * MAXB + j]
            keys = k_ref[block, :, rows]
            s = jnp.dot(keys, q2, preferred_element_type=jnp.float32) + b_ref[j]
            s_ref[j] = s
            high = jnp.maximum(high, jnp.max(s, axis=0, keepdims=True))
        total = jnp.zeros((1, wide), jnp.float32)
        acc = jnp.zeros((LANES, wide), jnp.float32)
        for j in range(MAXB):
            block = ids_ref[tile * MAXB + j]
            w = jnp.exp(s_ref[j] - high)
            total = total + jnp.sum(w, axis=0, keepdims=True)
            acc = acc + jnp.dot(
                vt_ref[block, rows, :], w.astype(jnp.bfloat16), preferred_element_type=jnp.float32
            )
        att_ref[slot, pl.ds(pair * LANES, HD), :] = (
            acc[:HD, :LANES] / total[:, :LANES]
        ).astype(jnp.bfloat16)
        att_ref[slot, pl.ds(pair * LANES + HD, HD), :] = (
            acc[HD:, LANES:] / total[:, LANES:]
        ).astype(jnp.bfloat16)

    @pl.when(tile == tiles - 1)
    def _():
        finish(lat_ref, att_ref[slot], w_ref, ogain_ref, o_ref, tile)


def attend(
    kinds, local_ids, tile_blocks, counts, near_obs, table, key_gain, queries_t, latent,
    output_gain, output_weight,
):
    tiles = queries_t.shape[0]
    near = near_obs.shape[0]
    grid_spec = pltpu.PrefetchScalarGridSpec(
        num_scalar_prefetch=4,
        grid=(tiles,),
        in_specs=[
            pl.BlockSpec(near_obs.shape, lambda t, *_: (0, 0, 0)),
            pl.BlockSpec(table.shape, lambda t, *_: (0, 0)),
            pl.BlockSpec((1, D), lambda t, *_: (0, 0)),
            pl.BlockSpec((1, D, CELLS), lambda t, *_: (t, 0, 0)),
            pl.BlockSpec(latent.shape, lambda t, *_: (0, 0)),
            pl.BlockSpec((1, D), lambda t, *_: (0, 0)),
            pl.BlockSpec(memory_space=pl.ANY),
        ],
        out_specs=pl.BlockSpec(latent.shape, lambda t, *_: (0, 0)),
        scratch_shapes=[
            pltpu.VMEM((near, OBS, D), jnp.bfloat16),
            pltpu.VMEM((near, D, OBS), jnp.bfloat16),
            pltpu.VMEM((MAXB, OBS, 2 * LANES), jnp.float32),
            pltpu.VMEM((MAXB, OBS, 2 * LANES), jnp.float32),
            pltpu.VMEM((2, D, CELLS), jnp.bfloat16),
            pltpu.VMEM((D, D), jnp.bfloat16),
            pltpu.SemaphoreType.DMA,
        ],
    )
    return pl.pallas_call(
        attend_kernel,
        grid_spec=grid_spec,
        out_shape=jax.ShapeDtypeStruct(latent.shape, jnp.bfloat16),
        compiler_params=pltpu.CompilerParams(
            dimension_semantics=("arbitrary",), vmem_limit_bytes=56 * 1024 * 1024
        ),
    )(
        kinds,
        local_ids.reshape(-1),
        tile_blocks,
        counts,
        near_obs,
        table,
        key_gain.reshape(1, D),
        queries_t,
        latent,
        output_gain.reshape(1, D),
        output_weight,
    )


def body(
    latent,
    query_gain,
    key_gain,
    output_gain,
    output_weight,
    observations,
    panels,
    instrument,
    observed_count,
    footprint,
    tile_blocks,
):
    block_count = observations.shape[0]
    position = lax.axis_index("lat")
    first_block = (position - 1) * block_count
    all_blocks = instrument.shape[0]
    table = lax.all_gather(panels, "lat", axis=0, tiled=True)
    kinds = table.shape[0] // CH
    near_obs = padded(observations, "lat", block_count)
    near_count = near_obs.shape[0]
    near_ids = jnp.clip(first_block + jnp.arange(near_count, dtype=jnp.int32), 0, all_blocks - 1)
    near_kinds = instrument[near_ids]
    counts = observed_count[near_ids]
    near_kinds = jnp.clip(near_kinds, 0, kinds - 1).astype(jnp.int32)
    tiles = latent.shape[0] // CELLS
    queries = (latent.astype(jnp.float32) * query_gain).astype(jnp.bfloat16)
    queries_t = jnp.swapaxes(queries.reshape(tiles, CELLS, D), 1, 2)
    local_ids = jnp.clip(footprint - first_block, 0, near_count - 1).astype(jnp.int32)
    return attend(
        near_kinds,
        local_ids,
        tile_blocks.astype(jnp.int32),
        counts,
        near_obs,
        table,
        key_gain.astype(jnp.float32),
        queries_t,
        latent,
        output_gain.astype(jnp.float32),
        output_weight,
    )


def solution(mesh):
    return jax.shard_map(
        body,
        mesh=mesh,
        in_specs=(
            P(("groups", "lat"), None),
            P(),
            P(),
            P(),
            P(),
            P(("groups", "lat"), None, None),
            P("lat", None),
            P("groups"),
            P("groups"),
            P(("groups", "lat"), None),
            P(("groups", "lat")),
        ),
        out_specs=P(("groups", "lat"), None),
        check_vma=False,
    )
```

```python
import math

import jax
import jax.numpy as jnp
from jax import lax
from jax.experimental import pallas as pl
from jax.experimental.pallas import tpu as pltpu
from jax.sharding import PartitionSpec as P

D = 1536
HD = 64
CH = 128
CELLS = 128
OBS = 128
MAXB = 6
LANES = 128


def padded(value, axis, width):
    peers, length = lax.axis_size(axis), value.shape[0]
    up = [(i, i + 1) for i in range(peers - 1)]
    down = [(j, i) for i, j in up]
    before = lax.ppermute(value[length - width:], axis, up)
    after = lax.ppermute(value[:width], axis, down)
    return jnp.concatenate([before, value, after], axis=0)


def normalize(values, gain):
    values = values.astype(jnp.float32)
    return values * lax.rsqrt(jnp.mean(values * values, axis=-1, keepdims=True) + 1e-06) * gain


def attend_kernel(
    kinds_ref, ids_ref, nb_ref, cnt_ref, obs_ref, table_ref, gain_ref, qt_ref, o_ref,
    k_ref, vt_ref, s_ref, b_ref, panel_ref, sem_ref,
):
    tile = pl.program_id(0)

    @pl.when(tile == 0)
    def _():
        copies = []
        for b in range(k_ref.shape[0]):
            start = pl.multiple_of(kinds_ref[b] * CH, CH)
            copy = pltpu.make_async_copy(
                table_ref.at[pl.ds(start, CH)], panel_ref.at[b], sem_ref.at[b]
            )
            copy.start()
            copies.append(copy)
        for b in range(k_ref.shape[0]):
            copies[b].wait()
            embedded = jnp.dot(obs_ref[b], panel_ref[b], preferred_element_type=jnp.float32)
            embedded = embedded.astype(jnp.bfloat16).astype(jnp.float32)
            norm = lax.rsqrt(jnp.mean(embedded * embedded, axis=1, keepdims=True) + 1e-06)
            k_ref[b] = (embedded * norm * gain_ref[...]).astype(jnp.bfloat16)
            vt_ref[b] = embedded.T.astype(jnp.bfloat16)

    used = nb_ref[tile]
    scale = 1.0 / math.sqrt(HD)
    row = lax.broadcasted_iota(jnp.int32, (LANES, 1), 0)
    low = row < HD
    wide = 2 * LANES
    for j in range(MAXB):
        keep = (row < cnt_ref[ids_ref[tile * MAXB + j]]) & (j < used)
        b_ref[j] = jnp.broadcast_to(jnp.where(keep, 0.0, -jnp.inf), (OBS, wide))
    for pair in range(D // LANES):
        rows = pl.ds(pair * LANES, LANES)
        qt = qt_ref[0, rows, :].astype(jnp.float32) * scale
        q2 = jnp.concatenate(
            [jnp.where(low, qt, 0.0), jnp.where(low, 0.0, qt)], axis=1
        ).astype(jnp.bfloat16)
        high = jnp.full((1, wide), -jnp.inf, jnp.float32)
        for j in range(MAXB):
            block = ids_ref[tile * MAXB + j]
            keys = k_ref[block, :, rows]
            s = jnp.dot(keys, q2, preferred_element_type=jnp.float32) + b_ref[j]
            s_ref[j] = s
            high = jnp.maximum(high, jnp.max(s, axis=0, keepdims=True))
        total = jnp.zeros((1, wide), jnp.float32)
        acc = jnp.zeros((LANES, wide), jnp.float32)
        for j in range(MAXB):
            block = ids_ref[tile * MAXB + j]
            w = jnp.exp(s_ref[j] - high)
            total = total + jnp.sum(w, axis=0, keepdims=True)
            acc = acc + jnp.dot(
                vt_ref[block, rows, :], w.astype(jnp.bfloat16), preferred_element_type=jnp.float32
            )
        o_ref[0, pl.ds(pair * LANES, HD), :] = (acc[:HD, :LANES] / total[:, :LANES]).astype(
            jnp.bfloat16
        )
        o_ref[0, pl.ds(pair * LANES + HD, HD), :] = (
            acc[HD:, LANES:] / total[:, LANES:]
        ).astype(jnp.bfloat16)


def attend(kinds, local_ids, tile_blocks, counts, near_obs, table, key_gain, queries_t):
    tiles = queries_t.shape[0]
    near = near_obs.shape[0]
    grid_spec = pltpu.PrefetchScalarGridSpec(
        num_scalar_prefetch=4,
        grid=(tiles,),
        in_specs=[
            pl.BlockSpec(near_obs.shape, lambda t, *_: (0, 0, 0)),
            pl.BlockSpec(memory_space=pl.ANY),
            pl.BlockSpec((1, D), lambda t, *_: (0, 0)),
            pl.BlockSpec((1, D, CELLS), lambda t, *_: (t, 0, 0)),
        ],
        out_specs=pl.BlockSpec((1, D, CELLS), lambda t, *_: (t, 0, 0)),
        scratch_shapes=[
            pltpu.VMEM((near, OBS, D), jnp.bfloat16),
            pltpu.VMEM((near, D, OBS), jnp.bfloat16),
            pltpu.VMEM((MAXB, OBS, 2 * LANES), jnp.float32),
            pltpu.VMEM((MAXB, OBS, 2 * LANES), jnp.float32),
            pltpu.VMEM((near, CH, D), jnp.bfloat16),
            pltpu.SemaphoreType.DMA((near,)),
        ],
    )
    return pl.pallas_call(
        attend_kernel,
        grid_spec=grid_spec,
        out_shape=jax.ShapeDtypeStruct(queries_t.shape, jnp.bfloat16),
        compiler_params=pltpu.CompilerParams(
            dimension_semantics=("arbitrary",), vmem_limit_bytes=48 * 1024 * 1024
        ),
    )(kinds, local_ids.reshape(-1), tile_blocks, counts, near_obs, table, key_gain.reshape(1, D), queries_t)


def body(
    latent,
    query_gain,
    key_gain,
    output_gain,
    output_weight,
    observations,
    panels,
    instrument,
    observed_count,
    footprint,
    tile_blocks,
):
    block_count = observations.shape[0]
    position = lax.axis_index("lat")
    first_block = (position - 1) * block_count
    all_blocks = instrument.shape[0]
    table = lax.all_gather(panels, "lat", axis=0, tiled=True)
    kinds = table.shape[0] // CH
    near_obs = padded(observations, "lat", block_count)
    near_count = near_obs.shape[0]
    near_ids = jnp.clip(first_block + jnp.arange(near_count, dtype=jnp.int32), 0, all_blocks - 1)
    near_kinds = instrument[near_ids]
    counts = observed_count[near_ids]
    near_kinds = jnp.clip(near_kinds, 0, kinds - 1).astype(jnp.int32)
    tiles = latent.shape[0] // CELLS
    queries = (latent.astype(jnp.float32) * query_gain).astype(jnp.bfloat16)
    queries_t = jnp.swapaxes(queries.reshape(tiles, CELLS, D), 1, 2)
    local_ids = jnp.clip(footprint - first_block, 0, near_count - 1).astype(jnp.int32)
    attended_t = attend(
        near_kinds,
        local_ids,
        tile_blocks.astype(jnp.int32),
        counts,
        near_obs,
        table,
        key_gain.astype(jnp.float32),
        queries_t,
    )
    projected = jnp.einsum(
        "tdq,de->tqe", attended_t, output_weight, preferred_element_type=jnp.float32
    ).reshape(tiles * CELLS, D)
    mixed = latent.astype(jnp.float32) + projected
    return normalize(mixed, output_gain).astype(jnp.bfloat16)


def solution(mesh):
    return jax.shard_map(
        body,
        mesh=mesh,
        in_specs=(
            P(("groups", "lat"), None),
            P(),
            P(),
            P(),
            P(),
            P(("groups", "lat"), None, None),
            P("lat", None),
            P("groups"),
            P("groups"),
            P(("groups", "lat"), None),
            P(("groups", "lat")),
        ),
        out_specs=P(("groups", "lat"), None),
        check_vma=False,
    )
```

```python
import math

import jax
import jax.numpy as jnp
from jax import lax
from jax.experimental import pallas as pl
from jax.experimental.pallas import tpu as pltpu
from jax.sharding import PartitionSpec as P

D = 1536
HD = 64
CH = 128
CELLS = 128
OBS = 128
MAXB = 6
LANES = 128


def padded(value, axis, width):
    peers, length = lax.axis_size(axis), value.shape[0]
    up = [(i, i + 1) for i in range(peers - 1)]
    down = [(j, i) for i, j in up]
    before = lax.ppermute(value[length - width:], axis, up)
    after = lax.ppermute(value[:width], axis, down)
    return jnp.concatenate([before, value, after], axis=0)


def normalize(values, gain):
    values = values.astype(jnp.float32)
    return values * lax.rsqrt(jnp.mean(values * values, axis=-1, keepdims=True) + 1e-06) * gain


def attend_kernel(
    kinds_ref, ids_ref, nb_ref, cnt_ref, obs_ref, table_ref, gain_ref, qt_ref, o_ref,
    k_ref, vt_ref, s_ref, b_ref,
):
    tile = pl.program_id(0)

    @pl.when(tile == 0)
    def _():
        for b in range(k_ref.shape[0]):
            start = pl.multiple_of(kinds_ref[b] * CH, CH)
            embedded = jnp.dot(
                obs_ref[b], table_ref[pl.ds(start, CH), :], preferred_element_type=jnp.float32
            )
            rounded = embedded.astype(jnp.bfloat16)
            vt_ref[b] = rounded.T
            embedded = rounded.astype(jnp.float32)
            norm = lax.rsqrt(jnp.mean(embedded * embedded, axis=1, keepdims=True) + 1e-06)
            k_ref[b] = (embedded * norm * gain_ref[...]).astype(jnp.bfloat16)

    used = nb_ref[tile]
    scale = 1.0 / math.sqrt(HD)
    row = lax.broadcasted_iota(jnp.int32, (LANES, 1), 0)
    low = row < HD
    wide = 2 * LANES
    for j in range(MAXB):
        keep = (row < cnt_ref[ids_ref[tile * MAXB + j]]) & (j < used)
        b_ref[j] = jnp.broadcast_to(jnp.where(keep, 0.0, -jnp.inf), (OBS, wide))
    for pair in range(D // LANES):
        rows = pl.ds(pair * LANES, LANES)
        qt = qt_ref[0, rows, :].astype(jnp.float32) * scale
        q2 = jnp.concatenate(
            [jnp.where(low, qt, 0.0), jnp.where(low, 0.0, qt)], axis=1
        ).astype(jnp.bfloat16)
        high = jnp.full((1, wide), -jnp.inf, jnp.float32)
        for j in range(MAXB):
            block = ids_ref[tile * MAXB + j]
            keys = k_ref[block, :, rows]
            s = jnp.dot(keys, q2, preferred_element_type=jnp.float32) + b_ref[j]
            s_ref[j] = s
            high = jnp.maximum(high, jnp.max(s, axis=0, keepdims=True))
        total = jnp.zeros((1, wide), jnp.float32)
        acc = jnp.zeros((LANES, wide), jnp.float32)
        for j in range(MAXB):
            block = ids_ref[tile * MAXB + j]
            w = jnp.exp(s_ref[j] - high)
            total = total + jnp.sum(w, axis=0, keepdims=True)
            acc = acc + jnp.dot(
                vt_ref[block, rows, :], w.astype(jnp.bfloat16), preferred_element_type=jnp.float32
            )
        o_ref[0, pl.ds(pair * LANES, HD), :] = (acc[:HD, :LANES] / total[:, :LANES]).astype(
            jnp.bfloat16
        )
        o_ref[0, pl.ds(pair * LANES + HD, HD), :] = (
            acc[HD:, LANES:] / total[:, LANES:]
        ).astype(jnp.bfloat16)


def attend(kinds, local_ids, tile_blocks, counts, near_obs, table, key_gain, queries_t):
    tiles = queries_t.shape[0]
    near = near_obs.shape[0]
    grid_spec = pltpu.PrefetchScalarGridSpec(
        num_scalar_prefetch=4,
        grid=(tiles,),
        in_specs=[
            pl.BlockSpec(near_obs.shape, lambda t, *_: (0, 0, 0)),
            pl.BlockSpec(table.shape, lambda t, *_: (0, 0)),
            pl.BlockSpec((1, D), lambda t, *_: (0, 0)),
            pl.BlockSpec((1, D, CELLS), lambda t, *_: (t, 0, 0)),
        ],
        out_specs=pl.BlockSpec((1, D, CELLS), lambda t, *_: (t, 0, 0)),
        scratch_shapes=[
            pltpu.VMEM((near, OBS, D), jnp.bfloat16),
            pltpu.VMEM((near, D, OBS), jnp.bfloat16),
            pltpu.VMEM((MAXB, OBS, 2 * LANES), jnp.float32),
            pltpu.VMEM((MAXB, OBS, 2 * LANES), jnp.float32),
        ],
    )
    return pl.pallas_call(
        attend_kernel,
        grid_spec=grid_spec,
        out_shape=jax.ShapeDtypeStruct(queries_t.shape, jnp.bfloat16),
        compiler_params=pltpu.CompilerParams(
            dimension_semantics=("arbitrary",), vmem_limit_bytes=48 * 1024 * 1024
        ),
    )(kinds, local_ids.reshape(-1), tile_blocks, counts, near_obs, table, key_gain.reshape(1, D), queries_t)


def body(
    latent,
    query_gain,
    key_gain,
    output_gain,
    output_weight,
    observations,
    panels,
    instrument,
    observed_count,
    footprint,
    tile_blocks,
):
    block_count = observations.shape[0]
    position = lax.axis_index("lat")
    first_block = (position - 1) * block_count
    all_blocks = instrument.shape[0]
    table = lax.all_gather(panels, "lat", axis=0, tiled=True)
    kinds = table.shape[0] // CH
    near_obs = padded(observations, "lat", block_count)
    near_count = near_obs.shape[0]
    near_ids = jnp.clip(first_block + jnp.arange(near_count, dtype=jnp.int32), 0, all_blocks - 1)
    near_kinds = instrument[near_ids]
    counts = observed_count[near_ids]
    near_kinds = jnp.clip(near_kinds, 0, kinds - 1).astype(jnp.int32)
    tiles = latent.shape[0] // CELLS
    queries = (latent.astype(jnp.float32) * query_gain).astype(jnp.bfloat16)
    queries_t = jnp.swapaxes(queries.reshape(tiles, CELLS, D), 1, 2)
    local_ids = jnp.clip(footprint - first_block, 0, near_count - 1).astype(jnp.int32)
    attended_t = attend(
        near_kinds,
        local_ids,
        tile_blocks.astype(jnp.int32),
        counts,
        near_obs,
        table,
        key_gain.astype(jnp.float32),
        queries_t,
    )
    projected = jnp.einsum(
        "tdq,de->tqe", attended_t, output_weight, preferred_element_type=jnp.float32
    ).reshape(tiles * CELLS, D)
    mixed = latent.astype(jnp.float32) + projected
    return normalize(mixed, output_gain).astype(jnp.bfloat16)


def solution(mesh):
    return jax.shard_map(
        body,
        mesh=mesh,
        in_specs=(
            P(("groups", "lat"), None),
            P(),
            P(),
            P(),
            P(),
            P(("groups", "lat"), None, None),
            P("lat", None),
            P("groups"),
            P("groups"),
            P(("groups", "lat"), None),
            P(("groups", "lat")),
        ),
        out_specs=P(("groups", "lat"), None),
        check_vma=False,
    )
```
